256 devices in a mesh: dp: 64 (over y, z, core), mp: 4 (over x).
Axes of the slice: x: 4, y: 4, z: 8, core: 2. Of those that a mesh axis runs over, the one named last changes fastest.
Arguments:
- queries: bfloat16 [32768, 1024], P('dp', 'mp'), may hold values from -20 to 20
- passages: bfloat16 [262144, 1024], P('dp', 'mp'), may hold values from -6 to 6
- positives: int32 [32768], P('dp'), may hold values from 0 to 4095, as said below
- negatives: int32 [64, 64], replicated, may hold values from -1 to 31, as said below
Outputs:
- losses: float32 [32768], P('dp')
- query_grad: float32 [32768, 1024], P('dp', 'mp')
- passage_grad: float32 [262144, 1024], P('dp', 'mp')
The draws below stay inside these ranges and needn't reach their ends.
Inputs may be any that keep to these rules, and one draw needn't show every extreme that they name: Within each dp index the 512 positives of its query block are distinct. `negatives`: each row names between 16 and 64 blocks (entries >= 0); some row names 64.
All inputs are finite; a program needn't handle non-finite values.
Results may differ from the reference program's by a relative error of at most 0.0075.
Values may be sent and summed in bfloat16 or wider, within the bound.
No kernel may reach another device: no remote copies, remote signals or barrier semaphores. Data moves between devices by JAX's collectives and lax.ppermute only.
A program may use at most 128 MiB of HBM per device.

```python
import jax
import jax.numpy as jnp
from jax import lax

D = 1024
QB = 512
PBS = 128
BLK_DEV = 32
CAND = 8704
N_DP = 64


def positive_table(key):
    base = jax.random.fold_in(key, 11)
    keys = jax.random.split(base, N_DP)
    rows = jax.vmap(lambda single: jax.random.permutation(single, PBS * BLK_DEV)[:QB])(keys)
    return rows.astype(jnp.int32)


def embed_pair(key):
    base = jax.random.fold_in(key, 37)
    key_pass, key_query = jax.random.split(base, 2)
    passages = jnp.clip(jax.random.normal(key_pass, (N_DP * PBS * BLK_DEV, D), jnp.float32), -6.0, 6.0)
    queries = jnp.clip(jax.random.normal(key_query, (N_DP * QB, D), jnp.float32), -6.0, 6.0)
    return (queries, passages)


def draw_queries(key, part):
    return embed_pair(key)[0].astype(jnp.bfloat16)


def draw_passages(key, part):
    return embed_pair(key)[1].astype(jnp.bfloat16)


def draw_positives(key, part):
    return positive_table(key).reshape(N_DP * QB)


def draw_negatives(key, part):
    base = jax.random.fold_in(key, 23)
    key_len, key_full, key_order, key_pick = jax.random.split(base, 4)
    lengths = jax.random.randint(key_len, (N_DP,), N_DP // 4, N_DP + 1)
    full_row = jax.random.randint(key_full, (), 0, N_DP)
    lengths = jnp.where(jnp.arange(N_DP) == full_row, N_DP, lengths)
    orders = jax.vmap(lambda single: jax.random.permutation(single, N_DP))(jax.random.split(key_order, N_DP))
    ranks = jnp.argsort(orders, axis=1, stable=True)
    present = ranks < lengths[:, None]
    picks = jax.random.randint(key_pick, (N_DP, N_DP), 0, BLK_DEV)
    return jnp.where(present, picks, -1).astype(jnp.int32)


def setup_inputs(seed: int = 0) -> dict:
    key_list = jax.random.split(jax.random.key(seed), 5)
    queries = draw_queries(jax.random.fold_in(key_list[4], 71), 0)
    passages = draw_passages(jax.random.fold_in(key_list[4], 71), 0)
    positives = draw_positives(jax.random.fold_in(key_list[4], 71), 0)
    negatives = draw_negatives(jax.random.fold_in(key_list[4], 71), 0)
    return dict(queries=queries, passages=passages, positives=positives, negatives=negatives)


def reference(queries, passages, positives, negatives):
    pass_dev = PBS * BLK_DEV
    factor = D ** -0.5
    blocks = passages.reshape(N_DP * BLK_DEV, PBS, D)
    owners = jnp.arange(N_DP, dtype=jnp.int32)
    inside = jnp.arange(PBS, dtype=jnp.int32)

    def one_block(carry, index):
        query_rows = lax.dynamic_slice_in_dim(queries, index * QB, QB, 0).astype(jnp.float32)
        chosen = lax.dynamic_slice_in_dim(positives, index * QB, QB, 0)
        global_pos = (index * pass_dev + chosen).astype(jnp.int32)
        wanted = lax.dynamic_index_in_dim(negatives, index, 0, keepdims=False)
        block_ids = (owners * BLK_DEV + jnp.maximum(wanted, 0)).astype(jnp.int32)
        negative_rows = jnp.take(blocks, block_ids, axis=0).reshape(N_DP * PBS, D)
        cands = jnp.concatenate([jnp.take(passages, global_pos, axis=0), negative_rows], 0).astype(jnp.float32)
        slot_ok = jnp.repeat(wanted >= 0, PBS)
        valid = jnp.concatenate([jnp.ones((QB,), bool), slot_ok], 0)
        scores = factor * jnp.dot(cands, query_rows.T)
        masked = jnp.where(valid[:, None], scores, jnp.float32(-1e30))
        top = jnp.max(masked, axis=0)
        total = jnp.sum(jnp.where(valid[:, None], jnp.exp(masked - top), jnp.float32(0.0)), axis=0)
        lse = top + jnp.log(total)
        own = jnp.diagonal(scores[:QB])
        loss = lse - own
        prob = jnp.where(valid[:, None], jnp.exp(masked - lse), jnp.float32(0.0))
        target = (jnp.arange(CAND)[:, None] == jnp.arange(QB)[None, :]).astype(jnp.float32)
        grad_scores = (prob - target).astype(jnp.bfloat16).astype(jnp.float32)
        query_grad = factor * jnp.dot(grad_scores.T, cands)
        cand_grad = factor * jnp.dot(grad_scores, query_rows)
        carry = carry.at[global_pos].add(cand_grad[:QB])
        neg_rows = (block_ids[:, None] * PBS + inside[None, :]).reshape(-1).astype(jnp.int32)
        carry = carry.at[neg_rows].add(cand_grad[QB:])
        return carry, (loss, query_grad)

    start = jnp.zeros((N_DP * pass_dev, D), jnp.float32)
    passage_grad, (losses, query_grad) = lax.scan(one_block, start, jnp.arange(N_DP, dtype=jnp.int32))
    return losses.reshape(N_DP * QB), query_grad.reshape(N_DP * QB, D), passage_grad
```

```python
import jax
import jax.numpy as jnp
from jax import lax
from jax.sharding import PartitionSpec as P

PBS = 128


def body(queries, passages, positives, negatives):
    dp_count = lax.axis_size("dp")
    mp_count = lax.axis_size("mp")
    own_index = lax.axis_index("dp")
    width_index = lax.axis_index("mp")
    query_rows, shard_width = queries.shape
    factor = (shard_width * mp_count) ** (-0.5)
    block_count = passages.shape[0] // PBS
    slots_per = dp_count // mp_count
    pos_per = query_rows // mp_count
    blocks = passages.reshape(block_count, PBS, shard_width)

    asked = lax.dynamic_index_in_dim(negatives, own_index, 1, keepdims=False)
    outgoing = jnp.take(blocks, jnp.maximum(asked, 0), axis=0)
    outgoing = jnp.where((asked >= 0)[:, None, None], outgoing, jnp.zeros_like(outgoing))
    fetched = lax.all_to_all(outgoing, "dp", split_axis=0, concat_axis=0, tiled=True)
    wanted = lax.dynamic_index_in_dim(negatives, own_index, 0, keepdims=False)

    positive_rows = jnp.take(passages, positives, axis=0)
    send = jnp.concatenate(
        [
            positive_rows.reshape(mp_count, pos_per, shard_width),
            fetched.reshape(mp_count, slots_per * PBS, shard_width),
        ],
        axis=1,
    )
    mine = lax.all_to_all(send, "mp", split_axis=0, concat_axis=0, tiled=True)
    row_count = mine.shape[1]
    q_full = lax.all_gather(queries, "mp", axis=1, tiled=True)
    q4 = q_full.reshape(query_rows, mp_count, shard_width)

    scores = factor * lax.dot_general(
        mine, q4, (((0, 2), (1, 2)), ((), ())), preferred_element_type=jnp.float32
    )

    rows = jnp.arange(row_count, dtype=jnp.int32)
    slot_of_row = width_index * slots_per + (rows - pos_per) // PBS
    slot_ok = jnp.take(wanted, jnp.clip(slot_of_row, 0, dp_count - 1)) >= 0
    valid = (rows < pos_per) | slot_ok
    target = (rows < pos_per)[:, None] & (
        (width_index * pos_per + rows)[:, None]
        == jnp.arange(query_rows, dtype=jnp.int32)[None, :]
    )

    masked = jnp.where(valid[:, None], scores, jnp.float32(-1e30))
    local_top = jnp.max(masked, axis=0)
    local_total = jnp.sum(
        jnp.where(valid[:, None], jnp.exp(masked - local_top), jnp.float32(0.0)), axis=0
    )
    local_own = jnp.sum(jnp.where(target, scores, jnp.float32(0.0)), axis=0)
    stats = lax.all_gather(jnp.stack([local_top, local_total, local_own]), "mp", axis=0)
    top = jnp.max(stats[:, 0], axis=0)
    total = jnp.sum(stats[:, 1] * jnp.exp(stats[:, 0] - top), axis=0)
    own_score = jnp.sum(stats[:, 2], axis=0)
    lse = top + jnp.log(total)
    losses = lse - own_score

    prob = jnp.where(valid[:, None], jnp.exp(masked - lse), jnp.float32(0.0))
    grad_scores = (prob - target.astype(jnp.float32)).astype(jnp.bfloat16)

    query_part = factor * lax.dot_general(
        grad_scores, mine, (((0,), (1,)), ((), ())), preferred_element_type=jnp.float32
    )
    query_grad = lax.psum_scatter(query_part, "mp", scatter_dimension=1, tiled=True)
    query_grad = query_grad.reshape(query_rows, shard_width)

    cand_grad = factor * jnp.dot(grad_scores, q_full, preferred_element_type=jnp.float32)
    cand_grad = cand_grad.reshape(row_count, mp_count, shard_width).transpose(1, 0, 2)
    pos_back = lax.all_to_all(
        cand_grad[:, :pos_per], "mp", split_axis=0, concat_axis=0, tiled=True
    ).reshape(query_rows, shard_width)
    neg_back = lax.all_to_all(
        cand_grad[:, pos_per:].astype(jnp.bfloat16), "mp", split_axis=0, concat_axis=0, tiled=True
    ).reshape(dp_count, PBS, shard_width)

    returned = lax.all_to_all(
        neg_back, "dp", split_axis=0, concat_axis=0, tiled=True
    ).astype(jnp.float32)
    selector = (asked[None, :] == jnp.arange(block_count, dtype=jnp.int32)[:, None]).astype(
        jnp.float32
    )
    block_grad = jnp.einsum("kr,rpd->kpd", selector, returned, precision=lax.Precision.HIGHEST)
    passage_grad = block_grad.reshape(block_count * PBS, shard_width).at[positives].add(pos_back)
    return (losses, query_grad, passage_grad)


def solution(mesh):
    in_specs = (P("dp", "mp"), P("dp", "mp"), P("dp"), P())
    out_specs = (P("dp"), P("dp", "mp"), P("dp", "mp"))
    return jax.shard_map(body, mesh=mesh, in_specs=in_specs, out_specs=out_specs, check_vma=False)
```

```python
import jax
import jax.numpy as jnp
from jax import lax
from jax.sharding import PartitionSpec as P

PBS = 128
HALVES = 2


def body(queries, passages, positives, negatives):
    dp_count = lax.axis_size("dp")
    mp_count = lax.axis_size("mp")
    own_index = lax.axis_index("dp")
    width_index = lax.axis_index("mp")
    query_rows, shard_width = queries.shape
    factor = (shard_width * mp_count) ** (-0.5)
    block_count = passages.shape[0] // PBS
    slots_per = dp_count // mp_count
    pos_per = query_rows // mp_count
    part = PBS // HALVES
    blocks = passages.reshape(block_count, PBS, shard_width)

    asked = lax.dynamic_index_in_dim(negatives, own_index, 1, keepdims=False)
    outgoing = jnp.take(blocks, jnp.maximum(asked, 0), axis=0)
    outgoing = jnp.where((asked >= 0)[:, None, None], outgoing, jnp.zeros_like(outgoing))
    wanted = lax.dynamic_index_in_dim(negatives, own_index, 0, keepdims=False)
    my_slots = lax.dynamic_slice_in_dim(wanted, width_index * slots_per, slots_per) >= 0

    q_full = lax.all_gather(queries, "mp", axis=1, tiled=True)
    q4 = q_full.reshape(query_rows, mp_count, shard_width)
    positive_rows = jnp.take(passages, positives, axis=0)

    mine, valid = [], []
    for h in range(HALVES):
        fetched = lax.all_to_all(
            outgoing[:, h * part:(h + 1) * part], "dp", split_axis=0, concat_axis=0, tiled=True
        )
        send = fetched.reshape(mp_count, slots_per * part, shard_width)
        ok = jnp.broadcast_to(my_slots[:, None], (slots_per, part)).reshape(-1)
        if h == 0:
            send = jnp.concatenate(
                [positive_rows.reshape(mp_count, pos_per, shard_width), send], axis=1
            )
            ok = jnp.concatenate([jnp.ones((pos_per,), bool), ok])
        mine.append(lax.all_to_all(send, "mp", split_axis=0, concat_axis=0, tiled=True))
        valid.append(ok)

    scores = [
        factor
        * lax.dot_general(c, q4, (((0, 2), (1, 2)), ((), ())), preferred_element_type=jnp.float32)
        for c in mine
    ]
    masked = [jnp.where(v[:, None], s, jnp.float32(-1e30)) for s, v in zip(scores, valid)]
    local_top = jnp.max(jnp.stack([jnp.max(x, axis=0) for x in masked]), axis=0)
    local_total = sum(
        jnp.sum(jnp.where(v[:, None], jnp.exp(x - local_top), jnp.float32(0.0)), axis=0)
        for x, v in zip(masked, valid)
    )
    target = (width_index * pos_per + jnp.arange(pos_per, dtype=jnp.int32))[:, None] == jnp.arange(
        query_rows, dtype=jnp.int32
    )[None, :]
    local_own = jnp.sum(jnp.where(target, scores[0][:pos_per], jnp.float32(0.0)), axis=0)
    stats = lax.all_gather(jnp.stack([local_top, local_total, local_own]), "mp", axis=0)
    top = jnp.max(stats[:, 0], axis=0)
    total = jnp.sum(stats[:, 1] * jnp.exp(stats[:, 0] - top), axis=0)
    own_score = jnp.sum(stats[:, 2], axis=0)
    lse = top + jnp.log(total)
    losses = lse - own_score

    grads = []
    for h in range(HALVES):
        prob = jnp.where(valid[h][:, None], jnp.exp(masked[h] - lse), jnp.float32(0.0))
        if h == 0:
            prob = jnp.concatenate([prob[:pos_per] - target.astype(jnp.float32), prob[pos_per:]])
        grads.append(prob.astype(jnp.bfloat16))

    query_part = sum(
        lax.dot_general(g, c, (((0,), (1,)), ((), ())), preferred_element_type=jnp.float32)
        for g, c in zip(grads, mine)
    )
    query_grad = lax.psum_scatter(factor * query_part, "mp", scatter_dimension=1, tiled=True)
    query_grad = query_grad.reshape(query_rows, shard_width)

    returned, pos_back = [], None
    for h in range(HALVES):
        cand = factor * jnp.dot(grads[h], q_full, preferred_element_type=jnp.float32)
        rows = cand.shape[0]
        pieces = []
        if h == 0:
            pos = cand[:pos_per]
            rounded = lax.reduce_precision(pos, exponent_bits=8, mantissa_bits=7)
            high = rounded.astype(jnp.bfloat16)
            low = (pos - rounded).astype(jnp.bfloat16)
            for x in (high, low):
                pieces.append(x.reshape(pos_per, mp_count, shard_width).transpose(1, 0, 2))
            cand = cand[pos_per:]
            rows -= pos_per
        neg = cand.astype(jnp.bfloat16).reshape(rows, mp_count, shard_width).transpose(1, 0, 2)
        pieces.append(neg)
        sent = lax.all_to_all(
            jnp.concatenate(pieces, axis=1), "mp", split_axis=0, concat_axis=0, tiled=True
        )
        if h == 0:
            pos_back = (
                sent[:, :pos_per].astype(jnp.float32) + sent[:, pos_per:2 * pos_per].astype(jnp.float32)
            ).reshape(query_rows, shard_width)
            sent = sent[:, 2 * pos_per:]
        back = lax.all_to_all(
            sent.reshape(dp_count, part, shard_width), "dp", split_axis=0, concat_axis=0, tiled=True
        )
        returned.append(back)
    returned = jnp.concatenate(returned, axis=1).astype(jnp.float32)

    selector = (asked[None, :] == jnp.arange(block_count, dtype=jnp.int32)[:, None]).astype(
        jnp.float32
    )
    block_grad = jnp.einsum("kr,rpd->kpd", selector, returned, precision=lax.Precision.HIGHEST)
    passage_grad = block_grad.reshape(block_count * PBS, shard_width).at[positives].add(pos_back)
    return (losses, query_grad, passage_grad)


def solution(mesh):
    in_specs = (P("dp", "mp"), P("dp", "mp"), P("dp"), P())
    out_specs = (P("dp"), P("dp", "mp"), P("dp", "mp"))
    return jax.shard_map(body, mesh=mesh, in_specs=in_specs, out_specs=out_specs, check_vma=False)
```

```python
import jax
import jax.numpy as jnp
from jax import lax
from jax.sharding import PartitionSpec as P

PBS = 128


def body(queries, passages, positives, negatives):
    dp_count = lax.axis_size("dp")
    mp_count = lax.axis_size("mp")
    own_index = lax.axis_index("dp")
    width_index = lax.axis_index("mp")
    query_rows, shard_width = queries.shape
    factor = (shard_width * mp_count) ** (-0.5)
    block_count = passages.shape[0] // PBS
    pos_per = query_rows // mp_count
    quarter = PBS // mp_count
    blocks = passages.reshape(block_count, PBS, shard_width)

    asked = lax.dynamic_index_in_dim(negatives, own_index, 1, keepdims=False)
    outgoing = jnp.take(blocks, jnp.maximum(asked, 0), axis=0)
    outgoing = jnp.where((asked >= 0)[:, None, None], outgoing, jnp.zeros_like(outgoing))
    fetched = lax.all_to_all(
        outgoing.reshape(dp_count * mp_count, quarter, shard_width),
        ("dp", "mp"),
        split_axis=0,
        concat_axis=0,
        tiled=True,
    )
    neg = fetched.reshape(dp_count, mp_count, quarter, shard_width)
    wanted = lax.dynamic_index_in_dim(negatives, own_index, 0, keepdims=False)
    slot_ok = (wanted >= 0)[:, None, None]

    q_full = lax.all_gather(queries, "mp", axis=1, tiled=True)
    q4 = q_full.reshape(query_rows, mp_count, shard_width)
    positive_rows = jnp.take(passages, positives, axis=0)
    pos_all = lax.all_gather(positive_rows, "mp", axis=1, tiled=True)
    pos_mine = lax.dynamic_slice_in_dim(pos_all, width_index * pos_per, pos_per, 0)

    pos_scores = factor * lax.dot_general(
        pos_mine, q_full, (((1,), (1,)), ((), ())), preferred_element_type=jnp.float32
    )
    neg_scores = factor * lax.dot_general(
        neg, q4, (((1, 3), (1, 2)), ((), ())), preferred_element_type=jnp.float32
    )
    masked = jnp.where(slot_ok, neg_scores, jnp.float32(-1e30))
    local_top = jnp.maximum(jnp.max(pos_scores, axis=0), jnp.max(masked, axis=(0, 1)))
    local_total = jnp.sum(jnp.exp(pos_scores - local_top), axis=0) + jnp.sum(
        jnp.where(slot_ok, jnp.exp(masked - local_top), jnp.float32(0.0)), axis=(0, 1)
    )
    target = (width_index * pos_per + jnp.arange(pos_per, dtype=jnp.int32))[:, None] == jnp.arange(
        query_rows, dtype=jnp.int32
    )[None, :]
    local_own = jnp.sum(jnp.where(target, pos_scores, jnp.float32(0.0)), axis=0)
    stats = lax.all_gather(jnp.stack([local_top, local_total, local_own]), "mp", axis=0)
    top = jnp.max(stats[:, 0], axis=0)
    total = jnp.sum(stats[:, 1] * jnp.exp(stats[:, 0] - top), axis=0)
    own_score = jnp.sum(stats[:, 2], axis=0)
    lse = top + jnp.log(total)
    losses = lse - own_score

    pos_grads = (jnp.exp(pos_scores - lse) - target.astype(jnp.float32)).astype(jnp.bfloat16)
    neg_grads = jnp.where(slot_ok, jnp.exp(masked - lse), jnp.float32(0.0)).astype(jnp.bfloat16)

    query_part = lax.dot_general(
        pos_grads,
        pos_mine.reshape(pos_per, mp_count, shard_width),
        (((0,), (0,)), ((), ())),
        preferred_element_type=jnp.float32,
    ) + lax.dot_general(
        neg_grads, neg, (((0, 1), (0, 2)), ((), ())), preferred_element_type=jnp.float32
    )
    query_grad = lax.psum_scatter(factor * query_part, "mp", scatter_dimension=1, tiled=True)
    query_grad = query_grad.reshape(query_rows, shard_width)

    cand_grad = factor * lax.dot_general(
        neg_grads, q4, (((2,), (0,)), ((), ())), preferred_element_type=jnp.float32
    )
    sending = cand_grad.astype(jnp.bfloat16).transpose(0, 2, 1, 3)
    returned = lax.all_to_all(
        sending.reshape(dp_count * mp_count, quarter, shard_width),
        ("dp", "mp"),
        split_axis=0,
        concat_axis=0,
        tiled=True,
    )
    returned = returned.reshape(dp_count, PBS, shard_width).astype(jnp.float32)

    all_pos_grads = lax.all_gather(pos_grads, "mp", axis=0, tiled=True)
    pos_back = factor * jnp.dot(all_pos_grads, queries, preferred_element_type=jnp.float32)

    selector = (asked[None, :] == jnp.arange(block_count, dtype=jnp.int32)[:, None]).astype(
        jnp.float32
    )
    block_grad = jnp.einsum("kr,rpd->kpd", selector, returned, precision=lax.Precision.HIGHEST)
    passage_grad = block_grad.reshape(block_count * PBS, shard_width).at[positives].add(pos_back)
    return (losses, query_grad, passage_grad)


def solution(mesh):
    in_specs = (P("dp", "mp"), P("dp", "mp"), P("dp"), P())
    out_specs = (P("dp"), P("dp", "mp"), P("dp", "mp"))
    return jax.shard_map(body, mesh=mesh, in_specs=in_specs, out_specs=out_specs, check_vma=False)
```

```python
import jax
import jax.numpy as jnp
from jax import lax
from jax.sharding import PartitionSpec as P

PBS = 128


def body(queries, passages, positives, negatives):
    dp_count = lax.axis_size("dp")
    mp_count = lax.axis_size("mp")
    own_index = lax.axis_index("dp")
    width_index = lax.axis_index("mp")
    query_rows, shard_width = queries.shape
    factor = (shard_width * mp_count) ** (-0.5)
    block_count = passages.shape[0] // PBS
    pos_per = query_rows // mp_count
    quarter = PBS // mp_count
    blocks = passages.reshape(block_count, PBS, shard_width)

    asked = lax.dynamic_index_in_dim(negatives, own_index, 1, keepdims=False)
    outgoing = jnp.take(blocks, jnp.maximum(asked, 0), axis=0)
    fetched = lax.all_to_all(
        outgoing.reshape(dp_count * mp_count, quarter, shard_width),
        ("dp", "mp"),
        split_axis=0,
        concat_axis=0,
        tiled=True,
    )
    neg = fetched.reshape(dp_count, mp_count, quarter, shard_width)
    wanted = lax.dynamic_index_in_dim(negatives, own_index, 0, keepdims=False)
    slot_ok = (wanted >= 0)[:, None, None]

    positive_rows = jnp.take(passages, positives, axis=0)
    both = lax.all_gather(
        jnp.concatenate([queries, positive_rows], axis=0), "mp", axis=1, tiled=True
    )
    q_full = both[:query_rows]
    q4 = q_full.reshape(query_rows, mp_count, shard_width)
    pos_mine = lax.dynamic_slice_in_dim(both, query_rows + width_index * pos_per, pos_per, 0)

    pos_scores = factor * lax.dot_general(
        pos_mine, q_full, (((1,), (1,)), ((), ())), preferred_element_type=jnp.float32
    )
    neg_scores = factor * lax.dot_general(
        neg, q4, (((1, 3), (1, 2)), ((), ())), preferred_element_type=jnp.float32
    )
    masked = jnp.where(slot_ok, neg_scores, jnp.float32(-1e30))
    local_top = jnp.maximum(jnp.max(pos_scores, axis=0), jnp.max(masked, axis=(0, 1)))
    local_total = jnp.sum(jnp.exp(pos_scores - local_top), axis=0) + jnp.sum(
        jnp.where(slot_ok, jnp.exp(masked - local_top), jnp.float32(0.0)), axis=(0, 1)
    )
    target = (width_index * pos_per + jnp.arange(pos_per, dtype=jnp.int32))[:, None] == jnp.arange(
        query_rows, dtype=jnp.int32
    )[None, :]
    local_own = jnp.sum(jnp.where(target, pos_scores, jnp.float32(0.0)), axis=0)
    stats = lax.all_gather(jnp.stack([local_top, local_total, local_own]), "mp", axis=0)
    top = jnp.max(stats[:, 0], axis=0)
    total = jnp.sum(stats[:, 1] * jnp.exp(stats[:, 0] - top), axis=0)
    own_score = jnp.sum(stats[:, 2], axis=0)
    lse = top + jnp.log(total)
    losses = lse - own_score

    pos_grads = (jnp.exp(pos_scores - lse) - target.astype(jnp.float32)).astype(jnp.bfloat16)
    neg_grads = jnp.where(slot_ok, jnp.exp(masked - lse), jnp.float32(0.0)).astype(jnp.bfloat16)

    query_part = lax.dot_general(
        pos_grads,
        pos_mine.reshape(pos_per, mp_count, shard_width),
        (((0,), (0,)), ((), ())),
        preferred_element_type=jnp.float32,
    ) + lax.dot_general(
        neg_grads, neg, (((0, 1), (0, 2)), ((), ())), preferred_element_type=jnp.float32
    )
    query_grad = lax.psum_scatter(factor * query_part, "mp", scatter_dimension=1, tiled=True)
    query_grad = query_grad.reshape(query_rows, shard_width)

    cand_grad = factor * lax.dot_general(
        neg_grads, q4, (((2,), (0,)), ((), ())), preferred_element_type=jnp.float32
    )
    sending = cand_grad.astype(jnp.bfloat16).transpose(0, 2, 1, 3)
    returned = lax.all_to_all(
        sending.reshape(dp_count * mp_count, quarter, shard_width),
        ("dp", "mp"),
        split_axis=0,
        concat_axis=0,
        tiled=True,
    )
    returned = returned.reshape(dp_count, PBS * shard_width)

    all_pos_grads = lax.all_gather(pos_grads, "mp", axis=0, tiled=True)
    pos_back = factor * jnp.dot(all_pos_grads, queries, preferred_element_type=jnp.float32)
    pos_part = jnp.zeros((block_count * PBS, shard_width), jnp.float32).at[positives].add(pos_back)
    returned, pos_part = lax.optimization_barrier((returned, pos_part))

    selector = (asked[None, :] == jnp.arange(block_count, dtype=jnp.int32)[:, None]).astype(
        jnp.bfloat16
    )
    block_grad = jnp.dot(selector, returned, preferred_element_type=jnp.float32)
    passage_grad = block_grad.reshape(block_count * PBS, shard_width) + pos_part
    return (losses, query_grad, passage_grad)


def solution(mesh):
    in_specs = (P("dp", "mp"), P("dp", "mp"), P("dp"), P())
    out_specs = (P("dp"), P("dp", "mp"), P("dp", "mp"))
    return jax.shard_map(body, mesh=mesh, in_specs=in_specs, out_specs=out_specs, check_vma=False)
```

```python
import jax
import jax.numpy as jnp
from jax import lax
from jax.sharding import PartitionSpec as P

PBS = 128


def body(queries, passages, positives, negatives):
    dp_count = lax.axis_size("dp")
    mp_count = lax.axis_size("mp")
    own_index = lax.axis_index("dp")
    width_index = lax.axis_index("mp")
    query_rows, shard_width = queries.shape
    factor = (shard_width * mp_count) ** (-0.5)
    block_count = passages.shape[0] // PBS
    pos_per = query_rows // mp_count
    quarter = PBS // mp_count
    blocks = passages.reshape(block_count, PBS, shard_width)

    asked = lax.dynamic_index_in_dim(negatives, own_index, 1, keepdims=False)
    outgoing = jnp.take(blocks, jnp.maximum(asked, 0), axis=0, mode="clip")
    fetched = lax.all_to_all(
        outgoing.reshape(dp_count * mp_count, quarter, shard_width),
        ("dp", "mp"),
        split_axis=0,
        concat_axis=0,
        tiled=True,
    )
    neg = fetched.reshape(dp_count, mp_count, quarter, shard_width)
    wanted = lax.dynamic_index_in_dim(negatives, own_index, 0, keepdims=False)
    slot_ok = (wanted >= 0)[:, None, None]

    positive_rows = jnp.take(passages, positives, axis=0, mode="clip")
    both = lax.all_gather(
        jnp.concatenate([queries, positive_rows], axis=0), "mp", axis=1, tiled=True
    )
    q_full = both[:query_rows]
    q4 = q_full.reshape(query_rows, mp_count, shard_width)
    pos_mine = lax.dynamic_slice_in_dim(both, query_rows + width_index * pos_per, pos_per, 0)

    pos_scores = factor * lax.dot_general(
        pos_mine, q_full, (((1,), (1,)), ((), ())), preferred_element_type=jnp.float32
    )
    neg_scores = factor * lax.dot_general(
        neg, q4, (((1, 3), (1, 2)), ((), ())), preferred_element_type=jnp.float32
    )
    masked = jnp.where(slot_ok, neg_scores, jnp.float32(-1e30))
    local_top = jnp.maximum(jnp.max(pos_scores, axis=0), jnp.max(masked, axis=(0, 1)))
    local_total = jnp.sum(jnp.exp(pos_scores - local_top), axis=0) + jnp.sum(
        jnp.where(slot_ok, jnp.exp(masked - local_top), jnp.float32(0.0)), axis=(0, 1)
    )
    target = (width_index * pos_per + jnp.arange(pos_per, dtype=jnp.int32))[:, None] == jnp.arange(
        query_rows, dtype=jnp.int32
    )[None, :]
    local_own = jnp.sum(jnp.where(target, pos_scores, jnp.float32(0.0)), axis=0)
    stats = lax.all_gather(jnp.stack([local_top, local_total, local_own]), "mp", axis=0)
    top = jnp.max(stats[:, 0], axis=0)
    total = jnp.sum(stats[:, 1] * jnp.exp(stats[:, 0] - top), axis=0)
    own_score = jnp.sum(stats[:, 2], axis=0)
    lse = top + jnp.log(total)
    losses = lse - own_score

    pos_grads = (jnp.exp(pos_scores - lse) - target.astype(jnp.float32)).astype(jnp.bfloat16)
    neg_grads = jnp.where(slot_ok, jnp.exp(masked - lse), jnp.float32(0.0)).astype(jnp.bfloat16)

    query_part = lax.dot_general(
        pos_grads,
        pos_mine.reshape(pos_per, mp_count, shard_width),
        (((0,), (0,)), ((), ())),
        preferred_element_type=jnp.float32,
    ) + lax.dot_general(
        neg_grads, neg, (((0, 1), (0, 2)), ((), ())), preferred_element_type=jnp.float32
    )
    query_grad = lax.psum_scatter(factor * query_part, "mp", scatter_dimension=1, tiled=True)
    query_grad = query_grad.reshape(query_rows, shard_width)

    cand_grad = factor * lax.dot_general(
        neg_grads, q4, (((2,), (0,)), ((), ())), preferred_element_type=jnp.float32
    )
    sending = cand_grad.astype(jnp.bfloat16).transpose(0, 2, 1, 3)
    returned = lax.all_to_all(
        sending.reshape(dp_count * mp_count, quarter, shard_width),
        ("dp", "mp"),
        split_axis=0,
        concat_axis=0,
        tiled=True,
    )
    returned = returned.reshape(dp_count, PBS, shard_width)

    all_pos_grads = lax.all_gather(pos_grads, "mp", axis=0, tiled=True)
    pos_back = factor * jnp.dot(all_pos_grads, queries, preferred_element_type=jnp.float32)
    pos_part = jnp.zeros((block_count * PBS, shard_width), jnp.float32).at[positives].add(pos_back)
    returned, pos_part = lax.optimization_barrier((returned, pos_part))

    selector = (asked[None, :] == jnp.arange(block_count, dtype=jnp.int32)[:, None]).astype(
        jnp.bfloat16
    )
    block_grad = jnp.einsum("kr,rpd->kpd", selector, returned, preferred_element_type=jnp.float32)
    passage_grad = block_grad.reshape(block_count * PBS, shard_width) + pos_part
    return (losses, query_grad, passage_grad)


def solution(mesh):
    in_specs = (P("dp", "mp"), P("dp", "mp"), P("dp"), P())
    out_specs = (P("dp"), P("dp", "mp"), P("dp", "mp"))
    return jax.shard_map(body, mesh=mesh, in_specs=in_specs, out_specs=out_specs, check_vma=False)
```

```python
import jax
import jax.numpy as jnp
from jax import lax
from jax.sharding import PartitionSpec as P

PBS = 128


def body(queries, passages, positives, negatives):
    dp_count = lax.axis_size("dp")
    mp_count = lax.axis_size("mp")
    own_index = lax.axis_index("dp")
    width_index = lax.axis_index("mp")
    query_rows, shard_width = queries.shape
    factor = (shard_width * mp_count) ** (-0.5)
    block_count = passages.shape[0] // PBS
    pos_per = query_rows // mp_count
    quarter = PBS // mp_count
    blocks = passages.reshape(block_count, PBS, shard_width)

    asked = lax.dynamic_index_in_dim(negatives, own_index, 1, keepdims=False)
    outgoing = jnp.take(blocks, jnp.maximum(asked, 0), axis=0, mode="clip")
    fetched = lax.all_to_all(
        outgoing.reshape(dp_count * mp_count, quarter, shard_width),
        ("dp", "mp"),
        split_axis=0,
        concat_axis=0,
        tiled=True,
    )
    neg = fetched.reshape(dp_count, mp_count, quarter, shard_width)
    wanted = lax.dynamic_index_in_dim(negatives, own_index, 0, keepdims=False)
    slot_ok = (wanted >= 0)[:, None, None]

    positive_rows = jnp.take(passages, positives, axis=0, mode="clip")
    both = lax.all_gather(
        jnp.concatenate([queries, positive_rows], axis=0), "mp", axis=1, tiled=True
    )
    q_full = both[:query_rows]
    q4 = q_full.reshape(query_rows, mp_count, shard_width)
    pos_mine = lax.dynamic_slice_in_dim(both, query_rows + width_index * pos_per, pos_per, 0)

    pos_scores = factor * lax.dot_general(
        pos_mine, q_full, (((1,), (1,)), ((), ())), preferred_element_type=jnp.float32
    )
    neg_scores = factor * lax.dot_general(
        neg, q4, (((1, 3), (1, 2)), ((), ())), preferred_element_type=jnp.float32
    )
    masked = jnp.where(slot_ok, neg_scores, jnp.float32(-1e30))
    local_top = jnp.maximum(jnp.max(pos_scores, axis=0), jnp.max(masked, axis=(0, 1)))
    local_total = jnp.sum(jnp.exp(pos_scores - local_top), axis=0) + jnp.sum(
        jnp.where(slot_ok, jnp.exp(masked - local_top), jnp.float32(0.0)), axis=(0, 1)
    )
    target = (width_index * pos_per + jnp.arange(pos_per, dtype=jnp.int32))[:, None] == jnp.arange(
        query_rows, dtype=jnp.int32
    )[None, :]
    local_own = jnp.sum(jnp.where(target, pos_scores, jnp.float32(0.0)), axis=0)
    stats = lax.all_gather(jnp.stack([local_top, local_total, local_own]), "mp", axis=0)
    top = jnp.max(stats[:, 0], axis=0)
    total = jnp.sum(stats[:, 1] * jnp.exp(stats[:, 0] - top), axis=0)
    own_score = jnp.sum(stats[:, 2], axis=0)
    lse = top + jnp.log(total)
    losses = lse - own_score

    pos_grads = (jnp.exp(pos_scores - lse) - target.astype(jnp.float32)).astype(jnp.bfloat16)
    neg_grads = jnp.where(slot_ok, jnp.exp(masked - lse), jnp.float32(0.0)).astype(jnp.bfloat16)

    query_part = lax.dot_general(
        pos_grads,
        pos_mine.reshape(pos_per, mp_count, shard_width),
        (((0,), (0,)), ((), ())),
        preferred_element_type=jnp.float32,
    ) + lax.dot_general(
        neg_grads, neg, (((0, 1), (0, 2)), ((), ())), preferred_element_type=jnp.float32
    )
    query_grad = lax.psum_scatter(factor * query_part, "mp", scatter_dimension=1, tiled=True)
    query_grad = query_grad.reshape(query_rows, shard_width)

    cand_grad = factor * lax.dot_general(
        neg_grads, q4, (((2,), (0,)), ((), ())), preferred_element_type=jnp.float32
    )
    sending = cand_grad.astype(jnp.bfloat16).transpose(0, 2, 1, 3)
    returned = lax.all_to_all(
        sending.reshape(dp_count * mp_count, quarter, shard_width),
        ("dp", "mp"),
        split_axis=0,
        concat_axis=0,
        tiled=True,
    )
    returned = returned.reshape(dp_count, PBS, shard_width)

    all_pos_grads = lax.all_gather(pos_grads, "mp", axis=0, tiled=True)
    pos_back = factor * jnp.dot(all_pos_grads, queries, preferred_element_type=jnp.float32)
    pos_part = jnp.zeros((block_count * PBS, shard_width), jnp.float32).at[positives].add(pos_back)
    returned, pos_part = lax.optimization_barrier((returned, pos_part))

    returned = jnp.where((asked >= 0)[:, None, None], returned.astype(jnp.float32), jnp.float32(0.0))
    passage_grad = (
        pos_part.reshape(block_count, PBS, shard_width)
        .at[jnp.maximum(asked, 0)]
        .add(returned, mode="clip")
        .reshape(block_count * PBS, shard_width)
    )
    return (losses, query_grad, passage_grad)


def solution(mesh):
    in_specs = (P("dp", "mp"), P("dp", "mp"), P("dp"), P())
    out_specs = (P("dp"), P("dp", "mp"), P("dp", "mp"))
    return jax.shard_map(body, mesh=mesh, in_specs=in_specs, out_specs=out_specs, check_vma=False)
```

```python
import jax
import jax.numpy as jnp
from jax import lax
from jax.sharding import PartitionSpec as P

PBS = 128


def body(queries, passages, positives, negatives):
    dp_count = lax.axis_size("dp")
    mp_count = lax.axis_size("mp")
    own_index = lax.axis_index("dp")
    width_index = lax.axis_index("mp")
    query_rows, shard_width = queries.shape
    factor = (shard_width * mp_count) ** (-0.5)
    block_count = passages.shape[0] // PBS
    pos_per = query_rows // mp_count
    quarter = PBS // mp_count
    blocks = passages.reshape(block_count, PBS, shard_width)

    asked = lax.dynamic_index_in_dim(negatives, own_index, 1, keepdims=False)
    outgoing = jnp.take(blocks, jnp.maximum(asked, 0), axis=0, mode="clip")
    positive_rows = jnp.take(passages, positives, axis=0, mode="clip")
    both = lax.all_gather(
        jnp.concatenate([queries, positive_rows], axis=0), "mp", axis=1, tiled=True
    )
    outgoing, both = lax.optimization_barrier((outgoing, both))
    fetched = lax.all_to_all(
        outgoing.reshape(dp_count * mp_count, quarter, shard_width),
        ("dp", "mp"),
        split_axis=0,
        concat_axis=0,
        tiled=True,
    )
    neg = fetched.reshape(dp_count, mp_count, quarter, shard_width)
    wanted = lax.dynamic_index_in_dim(negatives, own_index, 0, keepdims=False)
    slot_ok = (wanted >= 0)[:, None, None]

    q_full = both[:query_rows]
    q4 = q_full.reshape(query_rows, mp_count, shard_width)
    pos_mine = lax.dynamic_slice_in_dim(both, query_rows + width_index * pos_per, pos_per, 0)

    pos_scores = factor * lax.dot_general(
        pos_mine, q_full, (((1,), (1,)), ((), ())), preferred_element_type=jnp.float32
    )
    neg_scores = factor * lax.dot_general(
        neg, q4, (((1, 3), (1, 2)), ((), ())), preferred_element_type=jnp.float32
    )
    masked = jnp.where(slot_ok, neg_scores, jnp.float32(-1e30))
    local_top = jnp.maximum(jnp.max(pos_scores, axis=0), jnp.max(masked, axis=(0, 1)))
    local_total = jnp.sum(jnp.exp(pos_scores - local_top), axis=0) + jnp.sum(
        jnp.where(slot_ok, jnp.exp(masked - local_top), jnp.float32(0.0)), axis=(0, 1)
    )
    target = (width_index * pos_per + jnp.arange(pos_per, dtype=jnp.int32))[:, None] == jnp.arange(
        query_rows, dtype=jnp.int32
    )[None, :]
    local_own = jnp.sum(jnp.where(target, pos_scores, jnp.float32(0.0)), axis=0)
    stats = lax.all_gather(jnp.stack([local_top, local_total, local_own]), "mp", axis=0)
    top = jnp.max(stats[:, 0], axis=0)
    total = jnp.sum(stats[:, 1] * jnp.exp(stats[:, 0] - top), axis=0)
    own_score = jnp.sum(stats[:, 2], axis=0)
    lse = top + jnp.log(total)
    losses = lse - own_score

    pos_grads = (jnp.exp(pos_scores - lse) - target.astype(jnp.float32)).astype(jnp.bfloat16)
    neg_grads = jnp.where(slot_ok, jnp.exp(masked - lse), jnp.float32(0.0)).astype(jnp.bfloat16)

    query_part = lax.dot_general(
        pos_grads,
        pos_mine.reshape(pos_per, mp_count, shard_width),
        (((0,), (0,)), ((), ())),
        preferred_element_type=jnp.float32,
    ) + lax.dot_general(
        neg_grads, neg, (((0, 1), (0, 2)), ((), ())), preferred_element_type=jnp.float32
    )
    query_grad = lax.psum_scatter(factor * query_part, "mp", scatter_dimension=1, tiled=True)
    query_grad = query_grad.reshape(query_rows, shard_width)

    cand_grad = factor * lax.dot_general(
        neg_grads, q4, (((2,), (0,)), ((), ())), preferred_element_type=jnp.float32
    )
    sending = cand_grad.astype(jnp.bfloat16).transpose(0, 2, 1, 3)
    returned = lax.all_to_all(
        sending.reshape(dp_count * mp_count, quarter, shard_width),
        ("dp", "mp"),
        split_axis=0,
        concat_axis=0,
        tiled=True,
    )
    returned = returned.reshape(dp_count, PBS, shard_width)

    all_pos_grads = lax.all_gather(pos_grads, "mp", axis=0, tiled=True)
    pos_back = factor * jnp.dot(all_pos_grads, queries, preferred_element_type=jnp.float32)
    pos_part = jnp.zeros((block_count * PBS, shard_width), jnp.float32).at[positives].add(pos_back)
    returned, pos_part = lax.optimization_barrier((returned, pos_part))

    selector = (asked[None, :] == jnp.arange(block_count, dtype=jnp.int32)[:, None]).astype(
        jnp.bfloat16
    )
    block_grad = jnp.einsum("kr,rpd->kpd", selector, returned, preferred_element_type=jnp.float32)
    passage_grad = block_grad.reshape(block_count * PBS, shard_width) + pos_part
    return (losses, query_grad, passage_grad)


def solution(mesh):
    in_specs = (P("dp", "mp"), P("dp", "mp"), P("dp"), P())
    out_specs = (P("dp"), P("dp", "mp"), P("dp", "mp"))
    return jax.shard_map(body, mesh=mesh, in_specs=in_specs, out_specs=out_specs, check_vma=False)
```

```python
import jax
import jax.numpy as jnp
from jax import lax
from jax.sharding import PartitionSpec as P

PBS = 128


def body(queries, passages, positives, negatives):
    dp_count = lax.axis_size("dp")
    mp_count = lax.axis_size("mp")
    own_index = lax.axis_index("dp")
    width_index = lax.axis_index("mp")
    query_rows, shard_width = queries.shape
    factor = (shard_width * mp_count) ** (-0.5)
    block_count = passages.shape[0] // PBS
    pos_per = query_rows // mp_count
    quarter = PBS // mp_count
    blocks = passages.reshape(block_count, PBS, shard_width)

    asked = lax.dynamic_index_in_dim(negatives, own_index, 1, keepdims=False)
    outgoing = jnp.take(blocks, jnp.maximum(asked, 0), axis=0, mode="clip")
    fetched = lax.all_to_all(
        outgoing.reshape(dp_count * mp_count, quarter, shard_width),
        ("dp", "mp"),
        split_axis=0,
        concat_axis=0,
        tiled=True,
    )
    neg = fetched.reshape(dp_count, mp_count, quarter, shard_width)
    wanted = lax.dynamic_index_in_dim(negatives, own_index, 0, keepdims=False)
    slot_ok = (wanted >= 0)[:, None, None]

    positive_rows = jnp.take(passages, positives, axis=0, mode="clip")
    both = lax.all_gather(
        jnp.concatenate([queries, positive_rows], axis=0), "mp", axis=1, tiled=True
    )
    q_full = both[:query_rows]
    q4 = q_full.reshape(query_rows, mp_count, shard_width)
    pos_mine = lax.dynamic_slice_in_dim(both, query_rows + width_index * pos_per, pos_per, 0)

    pos_scores = factor * lax.dot_general(
        pos_mine, q_full, (((1,), (1,)), ((), ())), preferred_element_type=jnp.float32
    )
    neg_scores = factor * lax.dot_general(
        neg, q4, (((1, 3), (1, 2)), ((), ())), preferred_element_type=jnp.float32
    )
    masked = jnp.where(slot_ok, neg_scores, jnp.float32(-1e30))
    local_top = jnp.maximum(jnp.max(pos_scores, axis=0), jnp.max(masked, axis=(0, 1)))
    local_total = jnp.sum(jnp.exp(pos_scores - local_top), axis=0) + jnp.sum(
        jnp.where(slot_ok, jnp.exp(masked - local_top), jnp.float32(0.0)), axis=(0, 1)
    )
    target = (width_index * pos_per + jnp.arange(pos_per, dtype=jnp.int32))[:, None] == jnp.arange(
        query_rows, dtype=jnp.int32
    )[None, :]
    local_own = jnp.sum(jnp.where(target, pos_scores, jnp.float32(0.0)), axis=0)
    local = jnp.stack([local_top, local_total, local_own])
    got = jnp.stack(
        [local]
        + [
            lax.ppermute(local, "mp", [(i, (i + k) % mp_count) for i in range(mp_count)])
            for k in range(1, mp_count)
        ]
    )
    source_order = (width_index - jnp.arange(mp_count, dtype=jnp.int32)) % mp_count
    stats = jnp.take(got, source_order, axis=0, mode="clip")
    top = jnp.max(stats[:, 0], axis=0)
    total = jnp.sum(stats[:, 1] * jnp.exp(stats[:, 0] - top), axis=0)
    own_score = jnp.sum(stats[:, 2], axis=0)
    lse = top + jnp.log(total)
    losses = lse - own_score

    pos_grads = (jnp.exp(pos_scores - lse) - target.astype(jnp.float32)).astype(jnp.bfloat16)
    neg_grads = jnp.where(slot_ok, jnp.exp(masked - lse), jnp.float32(0.0)).astype(jnp.bfloat16)

    query_part = lax.dot_general(
        pos_grads,
        pos_mine.reshape(pos_per, mp_count, shard_width),
        (((0,), (0,)), ((), ())),
        preferred_element_type=jnp.float32,
    ) + lax.dot_general(
        neg_grads, neg, (((0, 1), (0, 2)), ((), ())), preferred_element_type=jnp.float32
    )
    query_grad = lax.psum_scatter(factor * query_part, "mp", scatter_dimension=1, tiled=True)
    query_grad = query_grad.reshape(query_rows, shard_width)

    cand_grad = factor * lax.dot_general(
        neg_grads, q4, (((2,), (0,)), ((), ())), preferred_element_type=jnp.float32
    )
    sending = cand_grad.astype(jnp.bfloat16).transpose(0, 2, 1, 3)
    returned = lax.all_to_all(
        sending.reshape(dp_count * mp_count, quarter, shard_width),
        ("dp", "mp"),
        split_axis=0,
        concat_axis=0,
        tiled=True,
    )
    returned = returned.reshape(dp_count, PBS, shard_width)

    all_pos_grads = lax.all_gather(pos_grads, "mp", axis=0, tiled=True)
    pos_back = factor * jnp.dot(all_pos_grads, queries, preferred_element_type=jnp.float32)
    pos_part = jnp.zeros((block_count * PBS, shard_width), jnp.float32).at[positives].add(pos_back)
    returned, pos_part = lax.optimization_barrier((returned, pos_part))

    selector = (asked[None, :] == jnp.arange(block_count, dtype=jnp.int32)[:, None]).astype(
        jnp.bfloat16
    )
    block_grad = jnp.einsum("kr,rpd->kpd", selector, returned, preferred_element_type=jnp.float32)
    passage_grad = block_grad.reshape(block_count * PBS, shard_width) + pos_part
    return (losses, query_grad, passage_grad)


def solution(mesh):
    in_specs = (P("dp", "mp"), P("dp", "mp"), P("dp"), P())
    out_specs = (P("dp"), P("dp", "mp"), P("dp", "mp"))
    return jax.shard_map(body, mesh=mesh, in_specs=in_specs, out_specs=out_specs, check_vma=False)
```

```python
import jax
import jax.numpy as jnp
from jax import lax
from jax.sharding import PartitionSpec as P

PBS = 128


def from_sources(payload, me, n):
    got = [payload(0)] + [
        lax.ppermute(payload(k), "mp", [(i, (i + k) % n) for i in range(n)]) for k in range(1, n)
    ]
    order = (me - jnp.arange(n, dtype=jnp.int32)) % n
    return jnp.take(jnp.stack(got), order, axis=0, mode="clip")


def body(queries, passages, positives, negatives):
    dp_count = lax.axis_size("dp")
    mp_count = lax.axis_size("mp")
    own_index = lax.axis_index("dp")
    width_index = lax.axis_index("mp")
    query_rows, shard_width = queries.shape
    factor = (shard_width * mp_count) ** (-0.5)
    block_count = passages.shape[0] // PBS
    pos_per = query_rows // mp_count
    quarter = PBS // mp_count
    blocks = passages.reshape(block_count, PBS, shard_width)

    asked = lax.dynamic_index_in_dim(negatives, own_index, 1, keepdims=False)
    outgoing = jnp.take(blocks, jnp.maximum(asked, 0), axis=0, mode="clip")
    fetched = lax.all_to_all(
        outgoing.reshape(dp_count * mp_count, quarter, shard_width),
        ("dp", "mp"),
        split_axis=0,
        concat_axis=0,
        tiled=True,
    )
    neg = fetched.reshape(dp_count, mp_count, quarter, shard_width)
    wanted = lax.dynamic_index_in_dim(negatives, own_index, 0, keepdims=False)
    slot_ok = (wanted >= 0)[:, None, None]

    positive_rows = jnp.take(passages, positives, axis=0, mode="clip")
    sources = from_sources(
        lambda k: jnp.concatenate(
            [
                queries,
                lax.dynamic_slice_in_dim(
                    positive_rows, ((width_index + k) % mp_count) * pos_per, pos_per, 0
                ),
            ],
            axis=0,
        ),
        width_index,
        mp_count,
    )
    q4 = sources[:, :query_rows].transpose(1, 0, 2)
    q_full = q4.reshape(query_rows, mp_count * shard_width)
    pos_mine = sources[:, query_rows:].transpose(1, 0, 2).reshape(pos_per, mp_count * shard_width)

    pos_scores = factor * lax.dot_general(
        pos_mine, q_full, (((1,), (1,)), ((), ())), preferred_element_type=jnp.float32
    )
    neg_scores = factor * lax.dot_general(
        neg, q4, (((1, 3), (1, 2)), ((), ())), preferred_element_type=jnp.float32
    )
    masked = jnp.where(slot_ok, neg_scores, jnp.float32(-1e30))
    local_top = jnp.maximum(jnp.max(pos_scores, axis=0), jnp.max(masked, axis=(0, 1)))
    local_total = jnp.sum(jnp.exp(pos_scores - local_top), axis=0) + jnp.sum(
        jnp.where(slot_ok, jnp.exp(masked - local_top), jnp.float32(0.0)), axis=(0, 1)
    )
    target = (width_index * pos_per + jnp.arange(pos_per, dtype=jnp.int32))[:, None] == jnp.arange(
        query_rows, dtype=jnp.int32
    )[None, :]
    local_own = jnp.sum(jnp.where(target, pos_scores, jnp.float32(0.0)), axis=0)
    local = jnp.stack([local_top, local_total, local_own])
    stats = from_sources(lambda k: local, width_index, mp_count)
    top = jnp.max(stats[:, 0], axis=0)
    total = jnp.sum(stats[:, 1] * jnp.exp(stats[:, 0] - top), axis=0)
    own_score = jnp.sum(stats[:, 2], axis=0)
    lse = top + jnp.log(total)
    losses = lse - own_score

    pos_grads = (jnp.exp(pos_scores - lse) - target.astype(jnp.float32)).astype(jnp.bfloat16)
    neg_grads = jnp.where(slot_ok, jnp.exp(masked - lse), jnp.float32(0.0)).astype(jnp.bfloat16)

    query_part = lax.dot_general(
        pos_grads,
        pos_mine.reshape(pos_per, mp_count, shard_width),
        (((0,), (0,)), ((), ())),
        preferred_element_type=jnp.float32,
    ) + lax.dot_general(
        neg_grads, neg, (((0, 1), (0, 2)), ((), ())), preferred_element_type=jnp.float32
    )
    query_part = factor * query_part
    query_grad = jnp.sum(
        from_sources(
            lambda k: lax.dynamic_index_in_dim(
                query_part, (width_index + k) % mp_count, 1, keepdims=False
            ),
            width_index,
            mp_count,
        ),
        axis=0,
    )

    cand_grad = factor * lax.dot_general(
        neg_grads, q4, (((2,), (0,)), ((), ())), preferred_element_type=jnp.float32
    )
    sending = cand_grad.astype(jnp.bfloat16).transpose(0, 2, 1, 3)
    returned = lax.all_to_all(
        sending.reshape(dp_count * mp_count, quarter, shard_width),
        ("dp", "mp"),
        split_axis=0,
        concat_axis=0,
        tiled=True,
    )
    returned = returned.reshape(dp_count, PBS, shard_width)

    all_pos_grads = from_sources(lambda k: pos_grads, width_index, mp_count).reshape(
        query_rows, query_rows
    )
    pos_back = factor * jnp.dot(all_pos_grads, queries, preferred_element_type=jnp.float32)
    pos_part = jnp.zeros((block_count * PBS, shard_width), jnp.float32).at[positives].add(pos_back)
    returned, pos_part = lax.optimization_barrier((returned, pos_part))

    selector = (asked[None, :] == jnp.arange(block_count, dtype=jnp.int32)[:, None]).astype(
        jnp.bfloat16
    )
    block_grad = jnp.einsum("kr,rpd->kpd", selector, returned, preferred_element_type=jnp.float32)
    passage_grad = block_grad.reshape(block_count * PBS, shard_width) + pos_part
    return (losses, query_grad, passage_grad)


def solution(mesh):
    in_specs = (P("dp", "mp"), P("dp", "mp"), P("dp"), P())
    out_specs = (P("dp"), P("dp", "mp"), P("dp", "mp"))
    return jax.shard_map(body, mesh=mesh, in_specs=in_specs, out_specs=out_specs, check_vma=False)
```

```python
import jax
import jax.numpy as jnp
from jax import lax
from jax.sharding import PartitionSpec as P

PBS = 128


def from_sources(payload, me, n):
    got = [payload(0)] + [
        lax.ppermute(payload(k), "mp", [(i, (i + k) % n) for i in range(n)]) for k in range(1, n)
    ]
    order = (me - jnp.arange(n, dtype=jnp.int32)) % n
    return jnp.take(jnp.stack(got), order, axis=0, mode="clip")


def body(queries, passages, positives, negatives):
    dp_count = lax.axis_size("dp")
    mp_count = lax.axis_size("mp")
    own_index = lax.axis_index("dp")
    width_index = lax.axis_index("mp")
    query_rows, shard_width = queries.shape
    factor = (shard_width * mp_count) ** (-0.5)
    block_count = passages.shape[0] // PBS
    pos_per = query_rows // mp_count
    quarter = PBS // mp_count
    blocks = passages.reshape(block_count, PBS, shard_width)

    asked = lax.dynamic_index_in_dim(negatives, own_index, 1, keepdims=False)
    outgoing = jnp.take(blocks, jnp.maximum(asked, 0), axis=0, mode="clip")
    fetched = lax.all_to_all(
        outgoing.reshape(dp_count * mp_count, quarter, shard_width),
        ("dp", "mp"),
        split_axis=0,
        concat_axis=0,
        tiled=True,
    )
    neg = fetched.reshape(dp_count, mp_count, quarter, shard_width)
    wanted = lax.dynamic_index_in_dim(negatives, own_index, 0, keepdims=False)
    slot_ok = (wanted >= 0)[:, None, None]

    positive_rows = jnp.take(passages, positives, axis=0, mode="clip")
    sources = from_sources(
        lambda k: jnp.concatenate(
            [
                queries,
                lax.dynamic_slice_in_dim(
                    positive_rows, ((width_index + k) % mp_count) * pos_per, pos_per, 0
                ),
            ],
            axis=0,
        ),
        width_index,
        mp_count,
    )
    q4 = sources[:, :query_rows].transpose(1, 0, 2)
    q_full = q4.reshape(query_rows, mp_count * shard_width)
    pos_mine = sources[:, query_rows:].transpose(1, 0, 2).reshape(pos_per, mp_count * shard_width)

    pos_scores = factor * lax.dot_general(
        pos_mine, q_full, (((1,), (1,)), ((), ())), preferred_element_type=jnp.float32
    )
    neg_scores = factor * lax.dot_general(
        neg, q4, (((1, 3), (1, 2)), ((), ())), preferred_element_type=jnp.float32
    )
    masked = jnp.where(slot_ok, neg_scores, jnp.float32(-1e30))
    local_top = jnp.maximum(jnp.max(pos_scores, axis=0), jnp.max(masked, axis=(0, 1)))
    local_total = jnp.sum(jnp.exp(pos_scores - local_top), axis=0) + jnp.sum(
        jnp.where(slot_ok, jnp.exp(masked - local_top), jnp.float32(0.0)), axis=(0, 1)
    )
    target = (width_index * pos_per + jnp.arange(pos_per, dtype=jnp.int32))[:, None] == jnp.arange(
        query_rows, dtype=jnp.int32
    )[None, :]
    local_own = jnp.sum(jnp.where(target, pos_scores, jnp.float32(0.0)), axis=0)
    local = jnp.stack([local_top, local_total, local_own])
    stats = from_sources(lambda k: local, width_index, mp_count)
    top = jnp.max(stats[:, 0], axis=0)
    total = jnp.sum(stats[:, 1] * jnp.exp(stats[:, 0] - top), axis=0)
    own_score = jnp.sum(stats[:, 2], axis=0)
    lse = top + jnp.log(total)
    losses = lse - own_score

    pos_grads = (jnp.exp(pos_scores - lse) - target.astype(jnp.float32)).astype(jnp.bfloat16)
    neg_grads = jnp.where(slot_ok, jnp.exp(masked - lse), jnp.float32(0.0)).astype(jnp.bfloat16)

    query_part = lax.dot_general(
        pos_grads,
        pos_mine.reshape(pos_per, mp_count, shard_width),
        (((0,), (0,)), ((), ())),
        preferred_element_type=jnp.float32,
    ) + lax.dot_general(
        neg_grads, neg, (((0, 1), (0, 2)), ((), ())), preferred_element_type=jnp.float32
    )
    query_part = factor * query_part
    query_grad = jnp.sum(
        from_sources(
            lambda k: lax.dynamic_index_in_dim(
                query_part, (width_index + k) % mp_count, 1, keepdims=False
            ),
            width_index,
            mp_count,
        ),
        axis=0,
    )

    cand_grad = factor * lax.dot_general(
        neg_grads, q4, (((2,), (0,)), ((), ())), preferred_element_type=jnp.float32
    )
    sending = cand_grad.astype(jnp.bfloat16).transpose(0, 2, 1, 3)
    returned = lax.all_to_all(
        sending.reshape(dp_count * mp_count, quarter, shard_width),
        ("dp", "mp"),
        split_axis=0,
        concat_axis=0,
        tiled=True,
    )
    returned = returned.reshape(dp_count, PBS, shard_width)

    all_pos_grads = from_sources(lambda k: pos_grads, width_index, mp_count).reshape(
        query_rows, query_rows
    )
    pos_back = factor * jnp.dot(all_pos_grads, queries, preferred_element_type=jnp.float32)
    pos_part = jnp.zeros((block_count * PBS, shard_width), jnp.float32).at[positives].add(pos_back)
    returned, pos_part = lax.optimization_barrier((returned, pos_part))

    selector = (asked[None, :] == jnp.arange(block_count, dtype=jnp.int32)[:, None]).astype(
        jnp.bfloat16
    )
    block_grad = jnp.einsum("kr,rpd->kpd", selector, returned, preferred_element_type=jnp.float32)
    passage_grad = (block_grad + pos_part.reshape(block_count, PBS, shard_width)).reshape(
        block_count * PBS, shard_width
    )
    return (losses, query_grad, passage_grad)


def solution(mesh):
    in_specs = (P("dp", "mp"), P("dp", "mp"), P("dp"), P())
    out_specs = (P("dp"), P("dp", "mp"), P("dp", "mp"))
    return jax.shard_map(body, mesh=mesh, in_specs=in_specs, out_specs=out_specs, check_vma=False)
```

```python
import jax
import jax.numpy as jnp
from jax import lax
from jax.experimental import pallas as pl
from jax.experimental.pallas import tpu as pltpu
from jax.sharding import PartitionSpec as P

PBS = 128
PER = 8

def _segment_kernel(asked_ref, ret_ref, pos_ref, out_ref):
    step = pl.program_id(0)

    @pl.when(step == 0)
    def _():
        out_ref[...] = pos_ref[...]

    for t in range(PER):
        k = asked_ref[step * PER + t]

        @pl.when(k >= 0)
        def _():
            out_ref[k] = out_ref[k] + ret_ref[t].astype(jnp.float32)


def segment_add(asked, returned, pos_blocks):
    n, rows, width = returned.shape
    blocks = pos_blocks.shape[0]
    return pl.pallas_call(
        _segment_kernel,
        grid_spec=pltpu.PrefetchScalarGridSpec(
            num_scalar_prefetch=1,
            grid=(n // PER,),
            in_specs=[
                pl.BlockSpec((PER, rows, width), lambda i, a: (i, 0, 0)),
                pl.BlockSpec((blocks, rows, width), lambda i, a: (0, 0, 0)),
            ],
            out_specs=pl.BlockSpec((blocks, rows, width), lambda i, a: (0, 0, 0)),
        ),
        out_shape=jax.ShapeDtypeStruct(pos_blocks.shape, jnp.float32),
        compiler_params=pltpu.CompilerParams(dimension_semantics=("arbitrary",)),
        cost_estimate=pl.CostEstimate(flops=n * rows * width, transcendentals=0,
                                      bytes_accessed=returned.size * 2 + pos_blocks.size * 8),
    )(asked, returned, pos_blocks)


def from_sources(payload, me, n):
    got = [payload(0)] + [
        lax.ppermute(payload(k), "mp", [(i, (i + k) % n) for i in range(n)]) for k in range(1, n)
    ]
    order = (me - jnp.arange(n, dtype=jnp.int32)) % n
    return jnp.take(jnp.stack(got), order, axis=0, mode="clip")


def body(queries, passages, positives, negatives):
    dp_count = lax.axis_size("dp")
    mp_count = lax.axis_size("mp")
    own_index = lax.axis_index("dp")
    width_index = lax.axis_index("mp")
    query_rows, shard_width = queries.shape
    factor = (shard_width * mp_count) ** (-0.5)
    block_count = passages.shape[0] // PBS
    pos_per = query_rows // mp_count
    quarter = PBS // mp_count
    blocks = passages.reshape(block_count, PBS, shard_width)

    asked = lax.dynamic_index_in_dim(negatives, own_index, 1, keepdims=False)
    outgoing = jnp.take(blocks, jnp.maximum(asked, 0), axis=0, mode="clip")
    fetched = lax.all_to_all(
        outgoing.reshape(dp_count * mp_count, quarter, shard_width),
        ("dp", "mp"),
        split_axis=0,
        concat_axis=0,
        tiled=True,
    )
    neg = fetched.reshape(dp_count, mp_count, quarter, shard_width)
    wanted = lax.dynamic_index_in_dim(negatives, own_index, 0, keepdims=False)
    slot_ok = (wanted >= 0)[:, None, None]

    positive_rows = jnp.take(passages, positives, axis=0, mode="clip")
    sources = from_sources(
        lambda k: jnp.concatenate(
            [
                queries,
                lax.dynamic_slice_in_dim(
                    positive_rows, ((width_index + k) % mp_count) * pos_per, pos_per, 0
                ),
            ],
            axis=0,
        ),
        width_index,
        mp_count,
    )
    q4 = sources[:, :query_rows].transpose(1, 0, 2)
    q_full = q4.reshape(query_rows, mp_count * shard_width)
    pos_mine = sources[:, query_rows:].transpose(1, 0, 2).reshape(pos_per, mp_count * shard_width)

    pos_scores = factor * lax.dot_general(
        pos_mine, q_full, (((1,), (1,)), ((), ())), preferred_element_type=jnp.float32
    )
    neg_scores = factor * lax.dot_general(
        neg, q4, (((1, 3), (1, 2)), ((), ())), preferred_element_type=jnp.float32
    )
    masked = jnp.where(slot_ok, neg_scores, jnp.float32(-1e30))
    local_top = jnp.maximum(jnp.max(pos_scores, axis=0), jnp.max(masked, axis=(0, 1)))
    local_total = jnp.sum(jnp.exp(pos_scores - local_top), axis=0) + jnp.sum(
        jnp.where(slot_ok, jnp.exp(masked - local_top), jnp.float32(0.0)), axis=(0, 1)
    )
    target = (width_index * pos_per + jnp.arange(pos_per, dtype=jnp.int32))[:, None] == jnp.arange(
        query_rows, dtype=jnp.int32
    )[None, :]
    local_own = jnp.sum(jnp.where(target, pos_scores, jnp.float32(0.0)), axis=0)
    local = jnp.stack([local_top, local_total, local_own])
    stats = from_sources(lambda k: local, width_index, mp_count)
    top = jnp.max(stats[:, 0], axis=0)
    total = jnp.sum(stats[:, 1] * jnp.exp(stats[:, 0] - top), axis=0)
    own_score = jnp.sum(stats[:, 2], axis=0)
    lse = top + jnp.log(total)
    losses = lse - own_score

    pos_grads = (jnp.exp(pos_scores - lse) - target.astype(jnp.float32)).astype(jnp.bfloat16)
    neg_grads = jnp.where(slot_ok, jnp.exp(masked - lse), jnp.float32(0.0)).astype(jnp.bfloat16)

    query_part = lax.dot_general(
        pos_grads,
        pos_mine.reshape(pos_per, mp_count, shard_width),
        (((0,), (0,)), ((), ())),
        preferred_element_type=jnp.float32,
    ) + lax.dot_general(
        neg_grads, neg, (((0, 1), (0, 2)), ((), ())), preferred_element_type=jnp.float32
    )
    query_part = factor * query_part
    query_grad = jnp.sum(
        from_sources(
            lambda k: lax.dynamic_index_in_dim(
                query_part, (width_index + k) % mp_count, 1, keepdims=False
            ),
            width_index,
            mp_count,
        ),
        axis=0,
    )

    cand_grad = factor * lax.dot_general(
        neg_grads, q4, (((2,), (0,)), ((), ())), preferred_element_type=jnp.float32
    )
    sending = cand_grad.astype(jnp.bfloat16).transpose(0, 2, 1, 3)
    returned = lax.all_to_all(
        sending.reshape(dp_count * mp_count, quarter, shard_width),
        ("dp", "mp"),
        split_axis=0,
        concat_axis=0,
        tiled=True,
    )
    returned = returned.reshape(dp_count, PBS, shard_width)

    all_pos_grads = from_sources(lambda k: pos_grads, width_index, mp_count).reshape(
        query_rows, query_rows
    )
    pos_back = factor * jnp.dot(all_pos_grads, queries, preferred_element_type=jnp.float32)
    pos_part = jnp.zeros((block_count * PBS, shard_width), jnp.float32).at[positives].add(pos_back)
    returned, pos_part = lax.optimization_barrier((returned, pos_part))

    passage_grad = segment_add(
        asked, returned, pos_part.reshape(block_count, PBS, shard_width)
    ).reshape(block_count * PBS, shard_width)
    return (losses, query_grad, passage_grad)


def solution(mesh):
    in_specs = (P("dp", "mp"), P("dp", "mp"), P("dp"), P())
    out_specs = (P("dp"), P("dp", "mp"), P("dp", "mp"))
    return jax.shard_map(body, mesh=mesh, in_specs=in_specs, out_specs=out_specs, check_vma=False)
```

```python
import jax
import jax.numpy as jnp
from jax import lax
from jax.experimental import pallas as pl
from jax.experimental.pallas import tpu as pltpu
from jax.sharding import PartitionSpec as P

PBS = 128
PER = 16

def _segment_kernel(asked_ref, ret_ref, pos_ref, out_ref):
    step = pl.program_id(1)

    @pl.when(step == 0)
    def _():
        out_ref[...] = pos_ref[...]

    for t in range(PER):
        k = asked_ref[step * PER + t]

        @pl.when(k >= 0)
        def _():
            out_ref[k] = out_ref[k] + ret_ref[t].astype(jnp.float32)


def segment_add(asked, returned, pos_blocks):
    n, rows, width = returned.shape
    blocks = pos_blocks.shape[0]
    return pl.pallas_call(
        _segment_kernel,
        grid_spec=pltpu.PrefetchScalarGridSpec(
            num_scalar_prefetch=1,
            grid=(2, n // PER),
            in_specs=[
                pl.BlockSpec((PER, rows // 2, width), lambda h, i, a: (i, h, 0)),
                pl.BlockSpec((blocks, rows // 2, width), lambda h, i, a: (0, h, 0)),
            ],
            out_specs=pl.BlockSpec((blocks, rows // 2, width), lambda h, i, a: (0, h, 0)),
        ),
        out_shape=jax.ShapeDtypeStruct(pos_blocks.shape, jnp.float32),
        compiler_params=pltpu.CompilerParams(dimension_semantics=("arbitrary", "arbitrary")),
        cost_estimate=pl.CostEstimate(flops=n * rows * width, transcendentals=0,
                                      bytes_accessed=returned.size * 2 + pos_blocks.size * 8),
    )(asked, returned, pos_blocks)


def from_sources(payload, me, n):
    got = [payload(0)] + [
        lax.ppermute(payload(k), "mp", [(i, (i + k) % n) for i in range(n)]) for k in range(1, n)
    ]
    order = (me - jnp.arange(n, dtype=jnp.int32)) % n
    return jnp.take(jnp.stack(got), order, axis=0, mode="clip")


def body(queries, passages, positives, negatives):
    dp_count = lax.axis_size("dp")
    mp_count = lax.axis_size("mp")
    own_index = lax.axis_index("dp")
    width_index = lax.axis_index("mp")
    query_rows, shard_width = queries.shape
    factor = (shard_width * mp_count) ** (-0.5)
    block_count = passages.shape[0] // PBS
    pos_per = query_rows // mp_count
    quarter = PBS // mp_count
    blocks = passages.reshape(block_count, PBS, shard_width)

    asked = lax.dynamic_index_in_dim(negatives, own_index, 1, keepdims=False)
    outgoing = jnp.take(blocks, jnp.maximum(asked, 0), axis=0, mode="clip")
    fetched = lax.all_to_all(
        outgoing.reshape(dp_count * mp_count, quarter, shard_width),
        ("dp", "mp"),
        split_axis=0,
        concat_axis=0,
        tiled=True,
    )
    neg = fetched.reshape(dp_count, mp_count, quarter, shard_width)
    wanted = lax.dynamic_index_in_dim(negatives, own_index, 0, keepdims=False)
    slot_ok = (wanted >= 0)[:, None, None]

    positive_rows = jnp.take(passages, positives, axis=0, mode="clip")
    sources = from_sources(
        lambda k: jnp.concatenate(
            [
                queries,
                lax.dynamic_slice_in_dim(
                    positive_rows, ((width_index + k) % mp_count) * pos_per, pos_per, 0
                ),
            ],
            axis=0,
        ),
        width_index,
        mp_count,
    )
    q4 = sources[:, :query_rows].transpose(1, 0, 2)
    q_full = q4.reshape(query_rows, mp_count * shard_width)
    pos_mine = sources[:, query_rows:].transpose(1, 0, 2).reshape(pos_per, mp_count * shard_width)

    pos_scores = factor * lax.dot_general(
        pos_mine, q_full, (((1,), (1,)), ((), ())), preferred_element_type=jnp.float32
    )
    neg_scores = factor * lax.dot_general(
        neg, q4, (((1, 3), (1, 2)), ((), ())), preferred_element_type=jnp.float32
    )
    masked = jnp.where(slot_ok, neg_scores, jnp.float32(-1e30))
    local_top = jnp.maximum(jnp.max(pos_scores, axis=0), jnp.max(masked, axis=(0, 1)))
    local_total = jnp.sum(jnp.exp(pos_scores - local_top), axis=0) + jnp.sum(
        jnp.where(slot_ok, jnp.exp(masked - local_top), jnp.float32(0.0)), axis=(0, 1)
    )
    target = (width_index * pos_per + jnp.arange(pos_per, dtype=jnp.int32))[:, None] == jnp.arange(
        query_rows, dtype=jnp.int32
    )[None, :]
    local_own = jnp.sum(jnp.where(target, pos_scores, jnp.float32(0.0)), axis=0)
    local = jnp.stack([local_top, local_total, local_own])
    stats = from_sources(lambda k: local, width_index, mp_count)
    top = jnp.max(stats[:, 0], axis=0)
    total = jnp.sum(stats[:, 1] * jnp.exp(stats[:, 0] - top), axis=0)
    own_score = jnp.sum(stats[:, 2], axis=0)
    lse = top + jnp.log(total)
    losses = lse - own_score

    pos_grads = (jnp.exp(pos_scores - lse) - target.astype(jnp.float32)).astype(jnp.bfloat16)
    neg_grads = jnp.where(slot_ok, jnp.exp(masked - lse), jnp.float32(0.0)).astype(jnp.bfloat16)

    query_part = lax.dot_general(
        pos_grads,
        pos_mine.reshape(pos_per, mp_count, shard_width),
        (((0,), (0,)), ((), ())),
        preferred_element_type=jnp.float32,
    ) + lax.dot_general(
        neg_grads, neg, (((0, 1), (0, 2)), ((), ())), preferred_element_type=jnp.float32
    )
    query_part = factor * query_part
    query_grad = jnp.sum(
        from_sources(
            lambda k: lax.dynamic_index_in_dim(
                query_part, (width_index + k) % mp_count, 1, keepdims=False
            ),
            width_index,
            mp_count,
        ),
        axis=0,
    )

    cand_grad = factor * lax.dot_general(
        neg_grads, q4, (((2,), (0,)), ((), ())), preferred_element_type=jnp.float32
    )
    sending = cand_grad.astype(jnp.bfloat16).transpose(0, 2, 1, 3)
    returned = lax.all_to_all(
        sending.reshape(dp_count * mp_count, quarter, shard_width),
        ("dp", "mp"),
        split_axis=0,
        concat_axis=0,
        tiled=True,
    )
    returned = returned.reshape(dp_count, PBS, shard_width)

    all_pos_grads = from_sources(lambda k: pos_grads, width_index, mp_count).reshape(
        query_rows, query_rows
    )
    pos_back = factor * jnp.dot(all_pos_grads, queries, preferred_element_type=jnp.float32)
    pos_part = jnp.zeros((block_count * PBS, shard_width), jnp.float32).at[positives].add(pos_back)
    returned, pos_part = lax.optimization_barrier((returned, pos_part))

    passage_grad = segment_add(
        asked, returned, pos_part.reshape(block_count, PBS, shard_width)
    ).reshape(block_count * PBS, shard_width)
    return (losses, query_grad, passage_grad)


def solution(mesh):
    in_specs = (P("dp", "mp"), P("dp", "mp"), P("dp"), P())
    out_specs = (P("dp"), P("dp", "mp"), P("dp", "mp"))
    return jax.shard_map(body, mesh=mesh, in_specs=in_specs, out_specs=out_specs, check_vma=False)
```

```python
import jax
import jax.numpy as jnp
from jax import lax
from jax.experimental import pallas as pl
from jax.experimental.pallas import tpu as pltpu
from jax.sharding import PartitionSpec as P

PBS = 128
PER = 32

def _segment_kernel(asked_ref, ret_ref, pos_ref, out_ref):
    step = pl.program_id(0)

    @pl.when(step == 0)
    def _():
        out_ref[...] = pos_ref[...]

    for t in range(PER):
        k = asked_ref[step * PER + t]

        @pl.when(k >= 0)
        def _():
            out_ref[k] = out_ref[k] + ret_ref[t].astype(jnp.float32)


def segment_add(asked, returned, pos_blocks):
    n, rows, width = returned.shape
    blocks = pos_blocks.shape[0]
    return pl.pallas_call(
        _segment_kernel,
        grid_spec=pltpu.PrefetchScalarGridSpec(
            num_scalar_prefetch=1,
            grid=(n // PER,),
            in_specs=[
                pl.BlockSpec((PER, rows, width), lambda i, a: (i, 0, 0)),
                pl.BlockSpec((blocks, rows, width), lambda i, a: (0, 0, 0)),
            ],
            out_specs=pl.BlockSpec((blocks, rows, width), lambda i, a: (0, 0, 0)),
        ),
        out_shape=jax.ShapeDtypeStruct(pos_blocks.shape, jnp.float32),
        compiler_params=pltpu.CompilerParams(dimension_semantics=("arbitrary",)),
        cost_estimate=pl.CostEstimate(flops=n * rows * width, transcendentals=0,
                                      bytes_accessed=returned.size * 2 + pos_blocks.size * 8),
    )(asked, returned, pos_blocks)


def from_sources(payload, me, n):
    got = [payload(0)] + [
        lax.ppermute(payload(k), "mp", [(i, (i + k) % n) for i in range(n)]) for k in range(1, n)
    ]
    order = (me - jnp.arange(n, dtype=jnp.int32)) % n
    return jnp.take(jnp.stack(got), order, axis=0, mode="clip")


def body(queries, passages, positives, negatives):
    dp_count = lax.axis_size("dp")
    mp_count = lax.axis_size("mp")
    own_index = lax.axis_index("dp")
    width_index = lax.axis_index("mp")
    query_rows, shard_width = queries.shape
    factor = (shard_width * mp_count) ** (-0.5)
    block_count = passages.shape[0] // PBS
    pos_per = query_rows // mp_count
    quarter = PBS // mp_count
    blocks = passages.reshape(block_count, PBS, shard_width)

    asked = lax.dynamic_index_in_dim(negatives, own_index, 1, keepdims=False)
    outgoing = jnp.take(blocks, jnp.maximum(asked, 0), axis=0, mode="clip")
    fetched = lax.all_to_all(
        outgoing.reshape(dp_count * mp_count, quarter, shard_width),
        ("dp", "mp"),
        split_axis=0,
        concat_axis=0,
        tiled=True,
    )
    neg = fetched.reshape(dp_count, mp_count, quarter, shard_width)
    wanted = lax.dynamic_index_in_dim(negatives, own_index, 0, keepdims=False)
    slot_ok = (wanted >= 0)[:, None, None]

    positive_rows = jnp.take(passages, positives, axis=0, mode="clip")
    sources = from_sources(
        lambda k: jnp.concatenate(
            [
                queries,
                lax.dynamic_slice_in_dim(
                    positive_rows, ((width_index + k) % mp_count) * pos_per, pos_per, 0
                ),
            ],
            axis=0,
        ),
        width_index,
        mp_count,
    )
    q4 = sources[:, :query_rows].transpose(1, 0, 2)
    q_full = q4.reshape(query_rows, mp_count * shard_width)
    pos_mine = sources[:, query_rows:].transpose(1, 0, 2).reshape(pos_per, mp_count * shard_width)

    pos_scores = factor * lax.dot_general(
        pos_mine, q_full, (((1,), (1,)), ((), ())), preferred_element_type=jnp.float32
    )
    neg_scores = factor * lax.dot_general(
        neg, q4, (((1, 3), (1, 2)), ((), ())), preferred_element_type=jnp.float32
    )
    masked = jnp.where(slot_ok, neg_scores, jnp.float32(-1e30))
    local_top = jnp.maximum(jnp.max(pos_scores, axis=0), jnp.max(masked, axis=(0, 1)))
    local_total = jnp.sum(jnp.exp(pos_scores - local_top), axis=0) + jnp.sum(
        jnp.where(slot_ok, jnp.exp(masked - local_top), jnp.float32(0.0)), axis=(0, 1)
    )
    target = (width_index * pos_per + jnp.arange(pos_per, dtype=jnp.int32))[:, None] == jnp.arange(
        query_rows, dtype=jnp.int32
    )[None, :]
    local_own = jnp.sum(jnp.where(target, pos_scores, jnp.float32(0.0)), axis=0)
    local = jnp.stack([local_top, local_total, local_own])
    stats = from_sources(lambda k: local, width_index, mp_count)
    top = jnp.max(stats[:, 0], axis=0)
    total = jnp.sum(stats[:, 1] * jnp.exp(stats[:, 0] - top), axis=0)
    own_score = jnp.sum(stats[:, 2], axis=0)
    lse = top + jnp.log(total)
    losses = lse - own_score

    pos_grads = (jnp.exp(pos_scores - lse) - target.astype(jnp.float32)).astype(jnp.bfloat16)
    neg_grads = jnp.where(slot_ok, jnp.exp(masked - lse), jnp.float32(0.0)).astype(jnp.bfloat16)

    query_part = lax.dot_general(
        pos_grads,
        pos_mine.reshape(pos_per, mp_count, shard_width),
        (((0,), (0,)), ((), ())),
        preferred_element_type=jnp.float32,
    ) + lax.dot_general(
        neg_grads, neg, (((0, 1), (0, 2)), ((), ())), preferred_element_type=jnp.float32
    )
    query_part = factor * query_part
    query_grad = jnp.sum(
        from_sources(
            lambda k: lax.dynamic_index_in_dim(
                query_part, (width_index + k) % mp_count, 1, keepdims=False
            ),
            width_index,
            mp_count,
        ),
        axis=0,
    )

    cand_grad = factor * lax.dot_general(
        neg_grads, q4, (((2,), (0,)), ((), ())), preferred_element_type=jnp.float32
    )
    sending = cand_grad.astype(jnp.bfloat16).transpose(0, 2, 1, 3)
    returned = lax.all_to_all(
        sending.reshape(dp_count * mp_count, quarter, shard_width),
        ("dp", "mp"),
        split_axis=0,
        concat_axis=0,
        tiled=True,
    )
    returned = returned.reshape(dp_count, PBS, shard_width)

    all_pos_grads = from_sources(lambda k: pos_grads, width_index, mp_count).reshape(
        query_rows, query_rows
    )
    pos_back = factor * jnp.dot(all_pos_grads, queries, preferred_element_type=jnp.float32)
    pos_part = jnp.zeros((block_count * PBS, shard_width), jnp.float32).at[positives].add(pos_back)
    returned, pos_part = lax.optimization_barrier((returned, pos_part))

    passage_grad = segment_add(
        asked, returned, pos_part.reshape(block_count, PBS, shard_width)
    ).reshape(block_count * PBS, shard_width)
    return (losses, query_grad, passage_grad)


def solution(mesh):
    in_specs = (P("dp", "mp"), P("dp", "mp"), P("dp"), P())
    out_specs = (P("dp"), P("dp", "mp"), P("dp", "mp"))
    return jax.shard_map(body, mesh=mesh, in_specs=in_specs, out_specs=out_specs, check_vma=False)
```
